512 devices in a mesh: exp: 32 (over z, core), rep: 16 (over y, x).
Axes of the slice: x: 4, y: 4, z: 16, core: 2. Of those that a mesh axis runs over, the one named last changes fastest.
Arguments:
- tokens: bfloat16 [65536, 1536], P(('exp', 'rep')), may hold values from -6 to 6
- grad_out: bfloat16 [65536, 1536], P(('exp', 'rep')), may hold values from -6 to 6
- expert_ids: int32 [65536, 2], P(('exp', 'rep')), may hold values from 0 to 31, all different within a row; in each aligned block of 128 rows (0 to 127, 128 to 255, ...) at most 10 rows name the same one
- probs: bfloat16 [65536, 2], P(('exp', 'rep')), may hold values from 0.099609375 to 1
- w_gate: bfloat16 [32, 768, 1536], P('exp', 'rep'), may hold values from -0.15625 to 0.15625
- w_up: bfloat16 [32, 768, 1536], P('exp', 'rep'), may hold values from -0.15625 to 0.15625
- w_down: bfloat16 [32, 768, 1536], P('exp', 'rep'), may hold values from -0.21875 to 0.21875
Outputs:
- grad_tokens: bfloat16 [65536, 1536], P(('exp', 'rep'))
- grad_probs: float32 [65536, 2], P(('exp', 'rep'))
- grad_gate: float32 [32, 768, 1536], P('exp', 'rep')
- grad_up: float32 [32, 768, 1536], P('exp', 'rep')
- grad_down: float32 [32, 768, 1536], P('exp', 'rep')
The draws below stay inside these ranges and needn't reach their ends.
Inputs may be any that keep to these rules, and one draw needn't show every extreme that they name: `expert_ids`: each token names two different experts; among the 128 tokens of one device no expert is named more than 10 times, a bound that some block reaches.
All inputs are finite; a program needn't handle non-finite values.
Results may differ from the reference program's by a relative error of at most 0.007.
Values may be sent and summed in bfloat16 or wider, within the bound.
No kernel may reach another device: no remote copies, remote signals or barrier semaphores. Data moves between devices by JAX's collectives and lax.ppermute only.
A program may use at most 64 MiB of HBM per device.

```python
import math
import jax
import jax.numpy as jnp
import numpy as np
from jax import lax

D = 1536
H_WIN = 768
TOP = 2
TOK_DEV = 128
EXPERTS = 32
CAP = 10
TOKENS = 65536
N_REP = 16


def block_levels(rng, shape, pieces, low, top_value):
    factor_of, own = 1.0, jax.random.fold_in(rng, 6)
    for position, shards_of in pieces:
        draws = jnp.exp(jax.random.uniform(jax.random.fold_in(own, position), (shards_of,), jnp.float32, low / len(pieces), top_value / len(pieces)))
        factor_of = factor_of * jnp.repeat(draws, shape[position] // shards_of).reshape([-1 if axis == position else 1 for axis in range(len(shape))])
    return factor_of


def deal_out(own_key, own, number, rows, count, top, most, lean):
    sequence = jax.random.permutation(own_key, count)
    crowded, common = load_shares(count, rows * top, most, lean, True), load_shares(count, rows * top, most, lean, False)
    places = jnp.arange(count)

    def named(tallies, offset_by):
        used = int((tallies > 0).sum())
        fixed = max(1, used // 4)
        shifted = fixed + (places - fixed + offset_by * (used - fixed)) % max(1, count - fixed)
        return jnp.zeros((count,), jnp.int32).at[sequence[jnp.where(places < fixed, places, shifted)]].set(jnp.asarray(tallies, jnp.int32))

    tallies = jnp.where(number % 4 == 0, named(crowded, number // 4), named(common, number - number // 4 - 1))
    mixed = jax.random.permutation(jax.random.fold_in(own, 3), count)
    donor, sink = mixed[0:count // 2 * 2:2], mixed[1:count // 2 * 2:2]
    slack = jnp.minimum(tallies[donor] - 1, most - tallies[sink]) // 2
    slack = jnp.where((donor == sequence[0]) | (sink == sequence[0]) | (tallies[sink] == 0), 0, jnp.maximum(slack, 0))
    shifted = jax.random.randint(jax.random.fold_in(own, 4), (count // 2,), 0, 1 << 20) % (slack + 1)
    tallies = tallies.at[donor].add(-shifted).at[sink].add(shifted)
    labels = jnp.searchsorted(jnp.cumsum(tallies), jnp.arange(rows * top), side="right").astype(jnp.int32)
    grid = labels.reshape(top, rows).T
    grid = grid[jax.random.permutation(jax.random.fold_in(own, 1), rows)]
    offset_by = jax.random.randint(jax.random.fold_in(own, 2), (rows, 1), 0, top)
    return jnp.take_along_axis(grid, (jnp.arange(top)[None, :] + offset_by) % top, axis=1)


def load_shares(number_of, total, bound, lean, full):
    weights = [(1 << 20) // math.isqrt(rank ** lean) + 1 for rank in range(1, number_of + 1)]
    largest = bound if full else min(bound, max(-(-total // number_of), total * weights[0] // sum(weights)))
    least = 1 if total - largest >= number_of - 1 else 0
    counts, rest = [largest] + [least] * (number_of - 1), total - largest - least * (number_of - 1)
    while rest > 0:
        free = [i for i in range(1, number_of) if counts[i] < largest] or [i for i in range(1, number_of) if counts[i] < bound]
        whole, left = sum([weights[i] for i in free]), rest
        for i in free:
            extra = min(bound - counts[i], max(1, left * weights[i] // whole), rest)
            counts[i] = counts[i] + extra
            rest = rest - extra
    return np.array(counts)


def bell_draw(rng, dims, scale, most, cuts=(), held_as=jnp.bfloat16):
    entries = scale * jax.random.normal(rng, dims, jnp.float32)
    if cuts:
        entries = entries * block_levels(rng, dims, cuts, -0.22, 0.18)
    return jnp.clip(entries, -most, most).astype(held_as)


def setup_inputs(seed: int = 0) -> dict:
    splits = jax.random.split(jax.random.key(seed), 8)
    tokens = bell_draw(splits[0], (TOKENS, D), 1.0, 6.0, ((0, 512),))
    grad_out = bell_draw(splits[1], (TOKENS, D), 1.0, 6.0, ((0, 512),))
    expert_ids_keys = jax.random.split(jax.random.fold_in(splits[2], 1), TOKENS // TOK_DEV)
    expert_ids_turns = jax.random.permutation(jax.random.fold_in(splits[2], 3), TOKENS // TOK_DEV)
    expert_ids = jax.vmap(lambda own, number: deal_out(jax.random.fold_in(splits[2], 2), own, number, TOK_DEV, EXPERTS, TOP, CAP, 2))(expert_ids_keys, expert_ids_turns).reshape((TOKENS, TOP))
    probs = jnp.clip(0.099609375 + 0.9003906 * jax.random.uniform(splits[3], (TOKENS, TOP), jnp.float32) ** block_levels(splits[3], (TOKENS, TOP), ((0, 512),), -0.2, 0.2), 0.099609375, 1.0).astype(jnp.bfloat16)
    w_gate = bell_draw(splits[4], (EXPERTS, H_WIN, D), D ** -0.5, 0.15625, ((0, 32), (1, 16)))
    w_up = bell_draw(splits[5], (EXPERTS, H_WIN, D), D ** -0.5, 0.15625, ((0, 32), (1, 16)))
    w_down = bell_draw(splits[6], (EXPERTS, H_WIN, D), H_WIN ** -0.5, 0.21875, ((0, 32), (1, 16)))
    return {"tokens": tokens, "grad_out": grad_out, "expert_ids": expert_ids, "probs": probs, "w_gate": w_gate, "w_up": w_up, "w_down": w_down}


def reference(tokens, grad_out, expert_ids, probs, w_gate, w_up, w_down):
    token_total = tokens.shape[0]
    width = tokens.shape[1]
    blocks = token_total // TOK_DEV
    pair_total = 2 * token_total
    flat = expert_ids.reshape(-1).astype(jnp.int32)
    onehot = (flat[:, None] == jnp.arange(EXPERTS, dtype=jnp.int32)[None, :]).astype(jnp.int32)
    running = jnp.cumsum(onehot.reshape(blocks, 2 * TOK_DEV, EXPERTS), axis=1).reshape(pair_total, EXPERTS)
    ranks = jnp.sum((running - 1) * onehot, axis=1).astype(jnp.int32)
    owner = (jnp.arange(pair_total, dtype=jnp.int32) // (2 * TOK_DEV)).astype(jnp.int32)
    slot_of = (owner * CAP + ranks).astype(jnp.int32)
    table = jnp.full((EXPERTS, blocks * CAP), pair_total, dtype=jnp.int32)
    table = table.at[flat, slot_of].set(jnp.arange(pair_total, dtype=jnp.int32))
    token_rows = jnp.concatenate([tokens, jnp.zeros((1, width), tokens.dtype)], axis=0)
    grad_rows = jnp.concatenate([grad_out, jnp.zeros((1, width), grad_out.dtype)], axis=0)
    prob_flat = jnp.concatenate([probs.reshape(-1).astype(jnp.float32), jnp.zeros((1,), jnp.float32)])
    parity = ((jnp.arange(H_WIN, dtype=jnp.int32) // (H_WIN // N_REP)) % 2).astype(jnp.int32)

    def expert_step(carry, inputs):
        pair_grads, prob_grads = carry
        members, gate_w, up_w, down_w = inputs
        source = (members // 2).astype(jnp.int32)
        rows = token_rows[source]
        grads = grad_rows[source]
        weight = prob_flat[members][:, None]
        gate = jnp.dot(rows, gate_w.T, preferred_element_type=jnp.float32)
        up = jnp.dot(rows, up_w.T, preferred_element_type=jnp.float32)
        sig = jax.nn.sigmoid(gate)
        act = gate * sig
        hidden = act * up
        back = jnp.dot(grads, down_w.T, preferred_element_type=jnp.float32)
        d_gate = (weight * back * up * sig * (1.0 + gate * (1.0 - sig))).astype(jnp.bfloat16)
        d_up = (weight * back * act).astype(jnp.bfloat16)
        weighted = (weight * hidden).astype(jnp.bfloat16)
        row_total = jnp.zeros((rows.shape[0], width), jnp.float32)
        prob_total = jnp.zeros((rows.shape[0],), jnp.float32)
        for half in (0, 1):
            select = (parity == half)
            select_b = select.astype(jnp.bfloat16)[None, :]
            part = jnp.dot(d_gate * select_b, gate_w, preferred_element_type=jnp.float32) + jnp.dot(d_up * select_b, up_w, preferred_element_type=jnp.float32)
            part = lax.optimization_barrier(part.astype(jnp.bfloat16)).astype(jnp.float32)
            prob_half = jnp.sum(hidden * back * select.astype(jnp.float32)[None, :], axis=1)
            prob_half = lax.optimization_barrier(prob_half.astype(jnp.bfloat16)).astype(jnp.float32)
            row_total = row_total + part
            prob_total = prob_total + prob_half
        row_total = lax.optimization_barrier(row_total.astype(jnp.bfloat16)).astype(jnp.float32)
        prob_total = lax.optimization_barrier(prob_total.astype(jnp.bfloat16)).astype(jnp.float32)
        grad_g = jnp.dot(d_gate.T, rows, preferred_element_type=jnp.float32)
        grad_u = jnp.dot(d_up.T, rows, preferred_element_type=jnp.float32)
        grad_d = jnp.dot(weighted.T, grads, preferred_element_type=jnp.float32)
        pair_grads = pair_grads.at[members].add(row_total)
        prob_grads = prob_grads.at[members].add(prob_total)
        return (pair_grads, prob_grads), (grad_g, grad_u, grad_d)

    start = (jnp.zeros((pair_total + 1, width), jnp.float32), jnp.zeros((pair_total + 1,), jnp.float32))
    finals, stacked = lax.scan(expert_step, start, (table, w_gate, w_up, w_down))
    pair_grads, prob_grads = finals
    grad_tokens = pair_grads[:pair_total].reshape(token_total, 2, width).sum(axis=1).astype(jnp.bfloat16)
    grad_probs = prob_grads[:pair_total].reshape(token_total, 2)
    return (grad_tokens, grad_probs, stacked[0], stacked[1], stacked[2])
```

```python
import jax
import jax.numpy as jnp
from jax import lax
from jax.sharding import Mesh
from jax.sharding import PartitionSpec as P

LANE = 128


def swap_pair(value):
    return lax.ppermute(value, "rl", [(0, 1), (1, 0)])


def shards(tokens, grad_out, expert_ids, probs, w_gate, w_up, w_down):
    token_count = tokens.shape[0]
    width = tokens.shape[1]
    exp_count = lax.axis_size("exp")
    capacity = 5 * token_count // (2 * exp_count)
    slots = exp_count * capacity
    chosen = expert_ids.reshape(-1)
    onehot = (chosen[:, None] == jnp.arange(exp_count, dtype=jnp.int32)[None, :]).astype(jnp.int32)
    ranks = jnp.sum((jnp.cumsum(onehot, axis=0) - 1) * onehot, axis=1)
    slot_of = chosen * capacity + ranks
    routing = (slot_of[None, :] == jnp.arange(slots, dtype=jnp.int32)[:, None]).astype(jnp.bfloat16)
    token_routing = routing.reshape(slots, token_count, 2).sum(axis=2)
    prob_pairs = probs.reshape(-1, 1)

    moved = jnp.dot(
        token_routing, jnp.concatenate([tokens, grad_out], axis=1), preferred_element_type=jnp.float32
    ).astype(jnp.bfloat16)
    slot_probs = jnp.dot(routing, prob_pairs, preferred_element_type=jnp.float32).astype(jnp.bfloat16)
    prob_block = jnp.concatenate([slot_probs, jnp.zeros((slots, LANE - 1), jnp.bfloat16)], axis=1)
    send = jnp.concatenate([moved, prob_block], axis=1).reshape(exp_count, capacity, -1)
    arrived = lax.all_to_all(send, "exp", split_axis=0, concat_axis=0, tiled=True)
    arrived = arrived.reshape(slots, -1)
    joined = jnp.concatenate([arrived, swap_pair(arrived)], axis=0)

    stacked = jnp.concatenate([w_gate, w_up, w_down], axis=0)
    full = lax.all_gather(stacked, "rh", axis=1, tiled=True)
    gate_w = full[0]
    up_w = full[1]
    down_w = full[2]

    rows = joined[:, :width]
    grads = joined[:, width : 2 * width]
    weight = joined[:, 2 * width : 2 * width + 1].astype(jnp.float32)
    gate = jnp.dot(rows, gate_w.T, preferred_element_type=jnp.float32)
    up = jnp.dot(rows, up_w.T, preferred_element_type=jnp.float32)
    sig = jax.nn.sigmoid(gate)
    act = gate * sig
    hidden = act * up
    back = jnp.dot(grads, down_w.T, preferred_element_type=jnp.float32)
    prob_part = jnp.sum(hidden * back, axis=1, keepdims=True)
    d_gate = (weight * back * up * sig * (1.0 + gate * (1.0 - sig))).astype(jnp.bfloat16)
    d_up = (weight * back * act).astype(jnp.bfloat16)
    weighted = (weight * hidden).astype(jnp.bfloat16)
    partial_rows = jnp.dot(d_gate, gate_w, preferred_element_type=jnp.float32) + jnp.dot(
        d_up, up_w, preferred_element_type=jnp.float32
    )
    row_count = rows.shape[0]
    packed = jnp.concatenate(
        [
            partial_rows.astype(jnp.bfloat16),
            prob_part.astype(jnp.bfloat16),
            jnp.zeros((row_count, LANE - 1), jnp.bfloat16),
        ],
        axis=1,
    )
    local = jnp.stack(
        [
            jnp.dot(d_gate.T, rows, preferred_element_type=jnp.float32),
            jnp.dot(d_up.T, rows, preferred_element_type=jnp.float32),
            jnp.dot(weighted.T, grads, preferred_element_type=jnp.float32),
        ]
    )
    received = swap_pair(packed[slots:])
    summed = (packed[:slots].astype(jnp.float32) + received.astype(jnp.float32)).astype(jnp.bfloat16)
    returned = lax.all_to_all(
        summed.reshape(exp_count, capacity, -1), "exp", split_axis=0, concat_axis=0, tiled=True
    ).reshape(slots, -1)
    weight_grads = lax.psum_scatter(local, "rh", scatter_dimension=1, tiled=True)

    grad_tokens = jnp.dot(
        token_routing.T, returned[:, :width], preferred_element_type=jnp.float32
    ).astype(jnp.bfloat16)
    grad_probs = jnp.dot(
        routing.T, returned[:, width : width + 1], preferred_element_type=jnp.float32
    ).reshape(token_count, 2)
    return (grad_tokens, grad_probs, weight_grads[0:1], weight_grads[1:2], weight_grads[2:3])


def solution(mesh):
    exp_count = mesh.shape["exp"]
    rep_count = mesh.shape["rep"]
    view = Mesh(mesh.devices.reshape(exp_count, rep_count // 2, 2), ("exp", "rh", "rl"))
    rows_spec = P(("exp", "rh", "rl"), None)
    weight_spec = P("exp", ("rh", "rl"), None)
    in_specs = (rows_spec,) * 4 + (weight_spec,) * 3
    out_specs = (rows_spec, rows_spec, weight_spec, weight_spec, weight_spec)
    return jax.shard_map(shards, mesh=view, in_specs=in_specs, out_specs=out_specs, check_vma=False)
```

```python
import jax
import jax.numpy as jnp
from jax import lax
from jax.sharding import Mesh
from jax.sharding import PartitionSpec as P

LANE = 128


def swap_pair(value):
    return lax.ppermute(value, "rl", [(0, 1), (1, 0)])


def shards(tokens, grad_out, expert_ids, probs, w_gate, w_up, w_down):
    token_count = tokens.shape[0]
    width = tokens.shape[1]
    exp_count = lax.axis_size("exp")
    capacity = 5 * token_count // (2 * exp_count)
    slots = exp_count * capacity
    chosen = expert_ids.reshape(-1)
    onehot = (chosen[:, None] == jnp.arange(exp_count, dtype=jnp.int32)[None, :]).astype(jnp.int32)
    ranks = jnp.sum((jnp.cumsum(onehot, axis=0) - 1) * onehot, axis=1)
    slot_of = chosen * capacity + ranks
    routing = (slot_of[None, :] == jnp.arange(slots, dtype=jnp.int32)[:, None]).astype(jnp.bfloat16)
    token_routing = routing.reshape(slots, token_count, 2).sum(axis=2)
    prob_pairs = probs.reshape(-1, 1)

    slot_tokens = jnp.dot(token_routing, tokens, preferred_element_type=jnp.float32).astype(jnp.bfloat16)
    slot_grads = jnp.dot(token_routing, grad_out, preferred_element_type=jnp.float32).astype(jnp.bfloat16)
    slot_probs = jnp.dot(routing, prob_pairs, preferred_element_type=jnp.float32).astype(jnp.bfloat16)
    prob_block = jnp.concatenate([slot_probs, jnp.zeros((slots, LANE - 1), jnp.bfloat16)], axis=1)
    send_t = jnp.concatenate([slot_tokens, prob_block], axis=1).reshape(exp_count, capacity, -1)
    arrived_t = lax.all_to_all(send_t, "exp", split_axis=0, concat_axis=0, tiled=True).reshape(slots, -1)
    send_g = slot_grads.reshape(exp_count, capacity, -1)
    arrived_g = lax.all_to_all(send_g, "exp", split_axis=0, concat_axis=0, tiled=True).reshape(slots, -1)
    joined_t = jnp.concatenate([arrived_t, swap_pair(arrived_t)], axis=0)
    joined_g = jnp.concatenate([arrived_g, swap_pair(arrived_g)], axis=0)

    stacked = jnp.concatenate([w_gate, w_up, w_down], axis=0)
    full = lax.all_gather(stacked, "rh", axis=1, tiled=True)
    gate_w = full[0]
    up_w = full[1]
    down_w = full[2]

    rows = joined_t[:, :width]
    grads = joined_g
    weight = joined_t[:, width : width + 1].astype(jnp.float32)
    gate = jnp.dot(rows, gate_w.T, preferred_element_type=jnp.float32)
    up = jnp.dot(rows, up_w.T, preferred_element_type=jnp.float32)
    sig = jax.nn.sigmoid(gate)
    act = gate * sig
    hidden = act * up
    back = jnp.dot(grads, down_w.T, preferred_element_type=jnp.float32)
    prob_part = jnp.sum(hidden * back, axis=1, keepdims=True)
    d_gate = (weight * back * up * sig * (1.0 + gate * (1.0 - sig))).astype(jnp.bfloat16)
    d_up = (weight * back * act).astype(jnp.bfloat16)
    weighted = (weight * hidden).astype(jnp.bfloat16)
    partial_rows = jnp.dot(d_gate, gate_w, preferred_element_type=jnp.float32) + jnp.dot(
        d_up, up_w, preferred_element_type=jnp.float32
    )
    row_count = rows.shape[0]
    packed = jnp.concatenate(
        [
            partial_rows.astype(jnp.bfloat16),
            prob_part.astype(jnp.bfloat16),
            jnp.zeros((row_count, LANE - 1), jnp.bfloat16),
        ],
        axis=1,
    )
    grad_down = lax.psum_scatter(
        jnp.dot(weighted.T, grads, preferred_element_type=jnp.float32)[None], "rh", scatter_dimension=1, tiled=True
    )
    grad_gate = lax.psum_scatter(
        jnp.dot(d_gate.T, rows, preferred_element_type=jnp.float32)[None], "rh", scatter_dimension=1, tiled=True
    )
    grad_up = lax.psum_scatter(
        jnp.dot(d_up.T, rows, preferred_element_type=jnp.float32)[None], "rh", scatter_dimension=1, tiled=True
    )
    mine = packed[:slots].reshape(exp_count, capacity, -1)
    theirs = packed[slots:].reshape(exp_count, capacity, -1)
    half = capacity // 2
    pieces = []
    for lo, hi in ((0, half), (half, capacity)):
        received = swap_pair(theirs[:, lo:hi])
        summed = (mine[:, lo:hi].astype(jnp.float32) + received.astype(jnp.float32)).astype(jnp.bfloat16)
        pieces.append(lax.all_to_all(summed, "exp", split_axis=0, concat_axis=0, tiled=True))
    returned = jnp.concatenate(pieces, axis=1).reshape(slots, -1)

    grad_tokens = jnp.dot(
        token_routing.T, returned[:, :width], preferred_element_type=jnp.float32
    ).astype(jnp.bfloat16)
    grad_probs = jnp.dot(
        routing.T, returned[:, width : width + 1], preferred_element_type=jnp.float32
    ).reshape(token_count, 2)
    return (grad_tokens, grad_probs, grad_gate, grad_up, grad_down)


def solution(mesh):
    exp_count = mesh.shape["exp"]
    rep_count = mesh.shape["rep"]
    view = Mesh(mesh.devices.reshape(exp_count, rep_count // 2, 2), ("exp", "rh", "rl"))
    rows_spec = P(("exp", "rh", "rl"), None)
    weight_spec = P("exp", ("rh", "rl"), None)
    in_specs = (rows_spec,) * 4 + (weight_spec,) * 3
    out_specs = (rows_spec, rows_spec, weight_spec, weight_spec, weight_spec)
    return jax.shard_map(shards, mesh=view, in_specs=in_specs, out_specs=out_specs, check_vma=False)
```

```python
import jax
import jax.numpy as jnp
from jax import lax
from jax.sharding import Mesh
from jax.sharding import PartitionSpec as P

LANE = 128


def swap_pair(value):
    return lax.ppermute(value, "rl", [(0, 1), (1, 0)])


def exchange(blocks):
    shape = blocks.shape
    split = blocks.reshape((lax.axis_size("ez"), lax.axis_size("ec")) + shape[1:])
    split = lax.all_to_all(split, "ez", split_axis=0, concat_axis=0, tiled=True)
    split = lax.all_to_all(split, "ec", split_axis=1, concat_axis=1, tiled=True)
    return split.reshape(shape)


def shards(tokens, grad_out, expert_ids, probs, w_gate, w_up, w_down):
    token_count = tokens.shape[0]
    width = tokens.shape[1]
    exp_count = lax.axis_size("ez") * lax.axis_size("ec")
    capacity = 5 * token_count // (2 * exp_count)
    slots = exp_count * capacity
    chosen = expert_ids.reshape(-1)
    onehot = (chosen[:, None] == jnp.arange(exp_count, dtype=jnp.int32)[None, :]).astype(jnp.int32)
    ranks = jnp.sum((jnp.cumsum(onehot, axis=0) - 1) * onehot, axis=1)
    slot_of = chosen * capacity + ranks
    routing = (slot_of[None, :] == jnp.arange(slots, dtype=jnp.int32)[:, None]).astype(jnp.bfloat16)
    token_routing = routing.reshape(slots, token_count, 2).sum(axis=2)
    prob_pairs = probs.reshape(-1, 1)

    slot_tokens = jnp.dot(token_routing, tokens, preferred_element_type=jnp.float32).astype(jnp.bfloat16)
    slot_grads = jnp.dot(token_routing, grad_out, preferred_element_type=jnp.float32).astype(jnp.bfloat16)
    slot_probs = jnp.dot(routing, prob_pairs, preferred_element_type=jnp.float32).astype(jnp.bfloat16)
    prob_block = jnp.concatenate([slot_probs, jnp.zeros((slots, LANE - 1), jnp.bfloat16)], axis=1)
    send_t = jnp.concatenate([slot_tokens, prob_block], axis=1).reshape(exp_count, capacity, -1)
    arrived_t = exchange(send_t).reshape(slots, -1)
    send_g = slot_grads.reshape(exp_count, capacity, -1)
    arrived_g = exchange(send_g).reshape(slots, -1)
    joined_t = jnp.concatenate([arrived_t, swap_pair(arrived_t)], axis=0)
    joined_g = jnp.concatenate([arrived_g, swap_pair(arrived_g)], axis=0)

    stacked = jnp.concatenate([w_gate, w_up, w_down], axis=0)
    full = lax.all_gather(stacked, "rh", axis=1, tiled=True)
    gate_w = full[0]
    up_w = full[1]
    down_w = full[2]

    rows = joined_t[:, :width]
    grads = joined_g
    weight = joined_t[:, width : width + 1].astype(jnp.float32)
    gate = jnp.dot(rows, gate_w.T, preferred_element_type=jnp.float32)
    up = jnp.dot(rows, up_w.T, preferred_element_type=jnp.float32)
    sig = jax.nn.sigmoid(gate)
    act = gate * sig
    hidden = act * up
    back = jnp.dot(grads, down_w.T, preferred_element_type=jnp.float32)
    prob_part = jnp.sum(hidden * back, axis=1, keepdims=True)
    d_gate = (weight * back * up * sig * (1.0 + gate * (1.0 - sig))).astype(jnp.bfloat16)
    d_up = (weight * back * act).astype(jnp.bfloat16)
    weighted = (weight * hidden).astype(jnp.bfloat16)
    partial_rows = jnp.dot(d_gate, gate_w, preferred_element_type=jnp.float32) + jnp.dot(
        d_up, up_w, preferred_element_type=jnp.float32
    )
    row_count = rows.shape[0]
    packed = jnp.concatenate(
        [
            partial_rows.astype(jnp.bfloat16),
            prob_part.astype(jnp.bfloat16),
            jnp.zeros((row_count, LANE - 1), jnp.bfloat16),
        ],
        axis=1,
    )
    local = jnp.stack(
        [
            jnp.dot(d_gate.T, rows, preferred_element_type=jnp.float32),
            jnp.dot(d_up.T, rows, preferred_element_type=jnp.float32),
            jnp.dot(weighted.T, grads, preferred_element_type=jnp.float32),
        ]
    )
    weight_grads = lax.psum_scatter(local, "rh", scatter_dimension=1, tiled=True)
    mine = packed[:slots].reshape(exp_count, capacity, -1)
    theirs = packed[slots:].reshape(exp_count, capacity, -1)
    half = capacity // 2
    pieces = []
    for lo, hi in ((0, half), (half, capacity)):
        received = swap_pair(theirs[:, lo:hi])
        summed = (mine[:, lo:hi].astype(jnp.float32) + received.astype(jnp.float32)).astype(jnp.bfloat16)
        pieces.append(exchange(summed))
    returned = jnp.concatenate(pieces, axis=1).reshape(slots, -1)

    grad_tokens = jnp.dot(
        token_routing.T, returned[:, :width], preferred_element_type=jnp.float32
    ).astype(jnp.bfloat16)
    grad_probs = jnp.dot(
        routing.T, returned[:, width : width + 1], preferred_element_type=jnp.float32
    ).reshape(token_count, 2)
    return (grad_tokens, grad_probs, weight_grads[0:1], weight_grads[1:2], weight_grads[2:3])


def solution(mesh):
    exp_count = mesh.shape["exp"]
    rep_count = mesh.shape["rep"]
    view = Mesh(mesh.devices.reshape(exp_count // 2, 2, rep_count // 2, 2), ("ez", "ec", "rh", "rl"))
    rows_spec = P(("ez", "ec", "rh", "rl"), None)
    weight_spec = P(("ez", "ec"), ("rh", "rl"), None)
    in_specs = (rows_spec,) * 4 + (weight_spec,) * 3
    out_specs = (rows_spec, rows_spec, weight_spec, weight_spec, weight_spec)
    return jax.shard_map(shards, mesh=view, in_specs=in_specs, out_specs=out_specs, check_vma=False)
```

```python
import jax
import jax.numpy as jnp
from jax import lax
from jax.sharding import Mesh
from jax.sharding import PartitionSpec as P

LANE = 128


def swap_pair(value):
    return lax.ppermute(value, "rl", [(0, 1), (1, 0)])


def exchange(blocks):
    shape = blocks.shape
    split = blocks.reshape((lax.axis_size("ez"), lax.axis_size("ec")) + shape[1:])
    split = lax.all_to_all(split, "ez", split_axis=0, concat_axis=0, tiled=True)
    split = lax.all_to_all(split, "ec", split_axis=1, concat_axis=1, tiled=True)
    return split.reshape(shape)


def shards(tokens, grad_out, expert_ids, probs, w_gate, w_up, w_down):
    token_count = tokens.shape[0]
    width = tokens.shape[1]
    exp_count = lax.axis_size("ez") * lax.axis_size("ec")
    capacity = 5 * token_count // (2 * exp_count)
    slots = exp_count * capacity
    chosen = expert_ids.reshape(-1)
    onehot = (chosen[:, None] == jnp.arange(exp_count, dtype=jnp.int32)[None, :]).astype(jnp.int32)
    ranks = jnp.sum((jnp.cumsum(onehot, axis=0) - 1) * onehot, axis=1)
    slot_of = chosen * capacity + ranks
    routing = (slot_of[None, :] == jnp.arange(slots, dtype=jnp.int32)[:, None]).astype(jnp.bfloat16)
    token_routing = routing.reshape(slots, token_count, 2).sum(axis=2)
    prob_pairs = probs.reshape(-1, 1)

    slot_tokens = jnp.dot(token_routing, tokens, preferred_element_type=jnp.float32).astype(jnp.bfloat16)
    slot_grads = jnp.dot(token_routing, grad_out, preferred_element_type=jnp.float32).astype(jnp.bfloat16)
    slot_probs = jnp.dot(routing, prob_pairs, preferred_element_type=jnp.float32).astype(jnp.bfloat16)
    prob_block = jnp.concatenate([slot_probs, jnp.zeros((slots, LANE - 1), jnp.bfloat16)], axis=1)
    send = jnp.concatenate([slot_tokens, slot_grads, prob_block], axis=1).reshape(exp_count, capacity, -1)

    stacked = jnp.concatenate([w_gate, w_up, w_down], axis=0)
    full = lax.all_gather(stacked, "rh", axis=1, tiled=True)
    gate_w = full[0]
    up_w = full[1]
    down_w = full[2]

    half = capacity // 2
    pieces = []
    local = None
    for lo, hi in ((0, half), (half, capacity)):
        arrived = exchange(send[:, lo:hi]).reshape(exp_count * (hi - lo), -1)
        chunk_rows = arrived.shape[0]
        joined = jnp.concatenate([arrived, swap_pair(arrived)], axis=0)
        rows = joined[:, :width]
        grads = joined[:, width : 2 * width]
        weight = joined[:, 2 * width : 2 * width + 1].astype(jnp.float32)
        gate = jnp.dot(rows, gate_w.T, preferred_element_type=jnp.float32)
        up = jnp.dot(rows, up_w.T, preferred_element_type=jnp.float32)
        sig = jax.nn.sigmoid(gate)
        act = gate * sig
        hidden = act * up
        back = jnp.dot(grads, down_w.T, preferred_element_type=jnp.float32)
        prob_part = jnp.sum(hidden * back, axis=1, keepdims=True)
        d_gate = (weight * back * up * sig * (1.0 + gate * (1.0 - sig))).astype(jnp.bfloat16)
        d_up = (weight * back * act).astype(jnp.bfloat16)
        weighted = (weight * hidden).astype(jnp.bfloat16)
        partial_rows = jnp.dot(d_gate, gate_w, preferred_element_type=jnp.float32) + jnp.dot(
            d_up, up_w, preferred_element_type=jnp.float32
        )
        packed = jnp.concatenate(
            [
                partial_rows.astype(jnp.bfloat16),
                prob_part.astype(jnp.bfloat16),
                jnp.zeros((2 * chunk_rows, LANE - 1), jnp.bfloat16),
            ],
            axis=1,
        )
        part = jnp.stack(
            [
                jnp.dot(d_gate.T, rows, preferred_element_type=jnp.float32),
                jnp.dot(d_up.T, rows, preferred_element_type=jnp.float32),
                jnp.dot(weighted.T, grads, preferred_element_type=jnp.float32),
            ]
        )
        local = part if local is None else local + part
        received = swap_pair(packed[chunk_rows:])
        summed = (packed[:chunk_rows].astype(jnp.float32) + received.astype(jnp.float32)).astype(jnp.bfloat16)
        pieces.append(exchange(summed.reshape(exp_count, hi - lo, -1)))
    weight_grads = lax.psum_scatter(local, "rh", scatter_dimension=1, tiled=True)
    returned = jnp.concatenate(pieces, axis=1).reshape(slots, -1)

    grad_tokens = jnp.dot(
        token_routing.T, returned[:, :width], preferred_element_type=jnp.float32
    ).astype(jnp.bfloat16)
    grad_probs = jnp.dot(
        routing.T, returned[:, width : width + 1], preferred_element_type=jnp.float32
    ).reshape(token_count, 2)
    return (grad_tokens, grad_probs, weight_grads[0:1], weight_grads[1:2], weight_grads[2:3])


def solution(mesh):
    exp_count = mesh.shape["exp"]
    rep_count = mesh.shape["rep"]
    view = Mesh(mesh.devices.reshape(exp_count // 2, 2, rep_count // 2, 2), ("ez", "ec", "rh", "rl"))
    rows_spec = P(("ez", "ec", "rh", "rl"), None)
    weight_spec = P(("ez", "ec"), ("rh", "rl"), None)
    in_specs = (rows_spec,) * 4 + (weight_spec,) * 3
    out_specs = (rows_spec, rows_spec, weight_spec, weight_spec, weight_spec)
    return jax.shard_map(shards, mesh=view, in_specs=in_specs, out_specs=out_specs, check_vma=False)
```

```python
import jax
import jax.numpy as jnp
from jax import lax
from jax.sharding import Mesh
from jax.sharding import PartitionSpec as P

LANE = 128


def swap_pair(value):
    return lax.ppermute(value, "rl", [(0, 1), (1, 0)])


def exchange(blocks):
    shape = blocks.shape
    split = blocks.reshape((lax.axis_size("ez"), lax.axis_size("ec")) + shape[1:])
    split = lax.all_to_all(split, "ez", split_axis=0, concat_axis=0, tiled=True)
    split = lax.all_to_all(split, "ec", split_axis=1, concat_axis=1, tiled=True)
    return split.reshape(shape)


def shards(tokens, grad_out, expert_ids, probs, w_gate, w_up, w_down):
    token_count = tokens.shape[0]
    width = tokens.shape[1]
    exp_count = lax.axis_size("ez") * lax.axis_size("ec")
    capacity = 5 * token_count // (2 * exp_count)
    slots = exp_count * capacity
    chosen = expert_ids.reshape(-1)
    onehot = (chosen[:, None] == jnp.arange(exp_count, dtype=jnp.int32)[None, :]).astype(jnp.int32)
    ranks = jnp.sum((jnp.cumsum(onehot, axis=0) - 1) * onehot, axis=1)
    slot_of = chosen * capacity + ranks
    routing = (slot_of[None, :] == jnp.arange(slots, dtype=jnp.int32)[:, None]).astype(jnp.bfloat16)
    token_routing = routing.reshape(slots, token_count, 2).sum(axis=2)
    prob_pairs = probs.reshape(-1, 1)

    slot_tokens = jnp.dot(token_routing, tokens, preferred_element_type=jnp.float32).astype(jnp.bfloat16)
    slot_grads = jnp.dot(token_routing, grad_out, preferred_element_type=jnp.float32).astype(jnp.bfloat16)
    slot_probs = jnp.dot(routing, prob_pairs, preferred_element_type=jnp.float32).astype(jnp.bfloat16)
    prob_block = jnp.concatenate([slot_probs, jnp.zeros((slots, LANE - 1), jnp.bfloat16)], axis=1)
    send_t = jnp.concatenate([slot_tokens, prob_block], axis=1).reshape(exp_count, capacity, -1)
    arrived_t = exchange(send_t).reshape(slots, -1)
    send_g = slot_grads.reshape(exp_count, capacity, -1)
    arrived_g = exchange(send_g).reshape(slots, -1)
    joined_t = jnp.concatenate([arrived_t, swap_pair(arrived_t)], axis=0)
    joined_g = jnp.concatenate([arrived_g, swap_pair(arrived_g)], axis=0)

    stacked = jnp.concatenate([w_gate, w_up, w_down], axis=0)
    full = lax.all_gather(stacked, "rh", axis=1, tiled=True)
    gate_w = full[0]
    up_w = full[1]
    down_w = full[2]

    rows = joined_t[:, :width]
    grads = joined_g
    weight = joined_t[:, width : width + 1].astype(jnp.float32)
    gate = jnp.dot(rows, gate_w.T, preferred_element_type=jnp.float32)
    up = jnp.dot(rows, up_w.T, preferred_element_type=jnp.float32)
    sig = jax.nn.sigmoid(gate)
    act = gate * sig
    hidden = act * up
    back = jnp.dot(grads, down_w.T, preferred_element_type=jnp.float32)
    prob_part = jnp.sum(hidden * back, axis=1, keepdims=True)
    d_gate = (weight * back * up * sig * (1.0 + gate * (1.0 - sig))).astype(jnp.bfloat16)
    d_up = (weight * back * act).astype(jnp.bfloat16)
    weighted = (weight * hidden).astype(jnp.bfloat16)
    partial_rows = jnp.dot(d_gate, gate_w, preferred_element_type=jnp.float32) + jnp.dot(
        d_up, up_w, preferred_element_type=jnp.float32
    )
    row_count = rows.shape[0]
    packed = jnp.concatenate(
        [
            partial_rows.astype(jnp.bfloat16),
            prob_part.astype(jnp.bfloat16),
            jnp.zeros((row_count, LANE - 1), jnp.bfloat16),
        ],
        axis=1,
    )
    local = jnp.stack(
        [
            jnp.dot(d_gate.T, rows, preferred_element_type=jnp.float32),
            jnp.dot(d_up.T, rows, preferred_element_type=jnp.float32),
            jnp.dot(weighted.T, grads, preferred_element_type=jnp.float32),
        ]
    )
    weight_grads = lax.psum_scatter(local, "rh", scatter_dimension=1, tiled=True)
    received = swap_pair(packed[slots:])
    summed = (packed[:slots].astype(jnp.float32) + received.astype(jnp.float32)).astype(jnp.bfloat16)
    returned = exchange(summed.reshape(exp_count, capacity, -1)).reshape(slots, -1)

    grad_tokens = jnp.dot(
        token_routing.T, returned[:, :width], preferred_element_type=jnp.float32
    ).astype(jnp.bfloat16)
    grad_probs = jnp.dot(
        routing.T, returned[:, width : width + 1], preferred_element_type=jnp.float32
    ).reshape(token_count, 2)
    return (grad_tokens, grad_probs, weight_grads[0:1], weight_grads[1:2], weight_grads[2:3])


def solution(mesh):
    exp_count = mesh.shape["exp"]
    rep_count = mesh.shape["rep"]
    view = Mesh(mesh.devices.reshape(exp_count // 2, 2, rep_count // 2, 2), ("ez", "ec", "rh", "rl"))
    rows_spec = P(("ez", "ec", "rh", "rl"), None)
    weight_spec = P(("ez", "ec"), ("rh", "rl"), None)
    in_specs = (rows_spec,) * 4 + (weight_spec,) * 3
    out_specs = (rows_spec, rows_spec, weight_spec, weight_spec, weight_spec)
    return jax.shard_map(shards, mesh=view, in_specs=in_specs, out_specs=out_specs, check_vma=False)
```

```python
import jax
import jax.numpy as jnp
from jax import lax
from jax.sharding import Mesh
from jax.sharding import PartitionSpec as P

LANE = 128


def swap_pair(value):
    return lax.ppermute(value, "rl", [(0, 1), (1, 0)])


def exchange(blocks):
    shape = blocks.shape
    split = blocks.reshape((lax.axis_size("ez"), lax.axis_size("ec")) + shape[1:])
    split = lax.all_to_all(split, "ez", split_axis=0, concat_axis=0, tiled=True)
    split = lax.all_to_all(split, "ec", split_axis=1, concat_axis=1, tiled=True)
    return split.reshape(shape)


def shards(tokens, grad_out, expert_ids, probs, w_gate, w_up, w_down):
    token_count = tokens.shape[0]
    width = tokens.shape[1]
    exp_count = lax.axis_size("ez") * lax.axis_size("ec")
    capacity = 5 * token_count // (2 * exp_count)
    slots = exp_count * capacity
    chosen = expert_ids.reshape(-1)
    onehot = (chosen[:, None] == jnp.arange(exp_count, dtype=jnp.int32)[None, :]).astype(jnp.int32)
    ranks = jnp.sum((jnp.cumsum(onehot, axis=0) - 1) * onehot, axis=1)
    slot_of = chosen * capacity + ranks
    routing = (slot_of[None, :] == jnp.arange(slots, dtype=jnp.int32)[:, None]).astype(jnp.bfloat16)
    token_routing = routing.reshape(slots, token_count, 2).sum(axis=2)
    prob_pairs = probs.reshape(-1, 1)

    slot_tokens = jnp.dot(token_routing, tokens, preferred_element_type=jnp.float32).astype(jnp.bfloat16)
    slot_grads = jnp.dot(token_routing, grad_out, preferred_element_type=jnp.float32).astype(jnp.bfloat16)
    slot_probs = jnp.dot(routing, prob_pairs, preferred_element_type=jnp.float32).astype(jnp.bfloat16)
    prob_block = jnp.concatenate([slot_probs, jnp.zeros((slots, LANE - 1), jnp.bfloat16)], axis=1)
    send_t = jnp.concatenate([slot_tokens, prob_block], axis=1).reshape(exp_count, capacity, -1)
    arrived_t = exchange(send_t).reshape(slots, -1)
    send_g = slot_grads.reshape(exp_count, capacity, -1)
    arrived_g = exchange(send_g).reshape(slots, -1)

    stacked = jnp.concatenate([w_gate, w_up, w_down], axis=0)
    full = lax.all_gather(stacked, "rh", axis=1, tiled=True)
    gate_w = full[0]
    up_w = full[1]
    down_w = full[2]

    def block(arrived_rows, grads):
        rows = arrived_rows[:, :width]
        weight = arrived_rows[:, width : width + 1].astype(jnp.float32)
        gate = jnp.dot(rows, gate_w.T, preferred_element_type=jnp.float32)
        up = jnp.dot(rows, up_w.T, preferred_element_type=jnp.float32)
        sig = jax.nn.sigmoid(gate)
        act = gate * sig
        hidden = act * up
        back = jnp.dot(grads, down_w.T, preferred_element_type=jnp.float32)
        prob_part = jnp.sum(hidden * back, axis=1, keepdims=True)
        d_gate = (weight * back * up * sig * (1.0 + gate * (1.0 - sig))).astype(jnp.bfloat16)
        d_up = (weight * back * act).astype(jnp.bfloat16)
        weighted = (weight * hidden).astype(jnp.bfloat16)
        partial_rows = jnp.dot(d_gate, gate_w, preferred_element_type=jnp.float32) + jnp.dot(
            d_up, up_w, preferred_element_type=jnp.float32
        )
        packed = jnp.concatenate(
            [
                partial_rows.astype(jnp.bfloat16),
                prob_part.astype(jnp.bfloat16),
                jnp.zeros((rows.shape[0], LANE - 1), jnp.bfloat16),
            ],
            axis=1,
        )
        local = jnp.stack(
            [
                jnp.dot(d_gate.T, rows, preferred_element_type=jnp.float32),
                jnp.dot(d_up.T, rows, preferred_element_type=jnp.float32),
                jnp.dot(weighted.T, grads, preferred_element_type=jnp.float32),
            ]
        )
        return packed, local

    partner_t = swap_pair(arrived_t)
    partner_g = swap_pair(arrived_g)
    packed_own, local_own = block(arrived_t, arrived_g)
    packed_partner, local_partner = block(partner_t, partner_g)
    received = swap_pair(packed_partner)
    weight_grads = lax.psum_scatter(local_own + local_partner, "rh", scatter_dimension=1, tiled=True)
    summed = (packed_own.astype(jnp.float32) + received.astype(jnp.float32)).astype(jnp.bfloat16)
    returned = exchange(summed.reshape(exp_count, capacity, -1)).reshape(slots, -1)

    grad_tokens = jnp.dot(
        token_routing.T, returned[:, :width], preferred_element_type=jnp.float32
    ).astype(jnp.bfloat16)
    grad_probs = jnp.dot(
        routing.T, returned[:, width : width + 1], preferred_element_type=jnp.float32
    ).reshape(token_count, 2)
    return (grad_tokens, grad_probs, weight_grads[0:1], weight_grads[1:2], weight_grads[2:3])


def solution(mesh):
    exp_count = mesh.shape["exp"]
    rep_count = mesh.shape["rep"]
    view = Mesh(mesh.devices.reshape(exp_count // 2, 2, rep_count // 2, 2), ("ez", "ec", "rh", "rl"))
    rows_spec = P(("ez", "ec", "rh", "rl"), None)
    weight_spec = P(("ez", "ec"), ("rh", "rl"), None)
    in_specs = (rows_spec,) * 4 + (weight_spec,) * 3
    out_specs = (rows_spec, rows_spec, weight_spec, weight_spec, weight_spec)
    return jax.shard_map(shards, mesh=view, in_specs=in_specs, out_specs=out_specs, check_vma=False)
```

```python
import jax
import jax.numpy as jnp
from jax import lax
from jax.sharding import Mesh
from jax.sharding import PartitionSpec as P

LANE = 128


def swap_pair(value):
    return lax.ppermute(value, "rl", [(0, 1), (1, 0)])


def exchange(blocks):
    shape = blocks.shape
    split = blocks.reshape((lax.axis_size("ez"), lax.axis_size("ec")) + shape[1:])
    split = lax.all_to_all(split, "ez", split_axis=0, concat_axis=0, tiled=True)
    split = lax.all_to_all(split, "ec", split_axis=1, concat_axis=1, tiled=True)
    return split.reshape(shape)


def shards(tokens, grad_out, expert_ids, probs, w_gate, w_up, w_down):
    token_count = tokens.shape[0]
    width = tokens.shape[1]
    exp_count = lax.axis_size("ez") * lax.axis_size("ec")
    capacity = 5 * token_count // (2 * exp_count)
    slots = exp_count * capacity
    chosen = expert_ids.reshape(-1)
    onehot = (chosen[:, None] == jnp.arange(exp_count, dtype=jnp.int32)[None, :]).astype(jnp.int32)
    ranks = jnp.sum((jnp.cumsum(onehot, axis=0) - 1) * onehot, axis=1)
    slot_of = chosen * capacity + ranks
    routing = (slot_of[None, :] == jnp.arange(slots, dtype=jnp.int32)[:, None]).astype(jnp.bfloat16)
    token_routing = routing.reshape(slots, token_count, 2).sum(axis=2)
    prob_pairs = probs.reshape(-1, 1)

    slot_tokens = jnp.dot(token_routing, tokens, preferred_element_type=jnp.float32).astype(jnp.bfloat16)
    slot_grads = jnp.dot(token_routing, grad_out, preferred_element_type=jnp.float32).astype(jnp.bfloat16)
    slot_probs = jnp.dot(routing, prob_pairs, preferred_element_type=jnp.float32).astype(jnp.bfloat16)
    prob_block = jnp.concatenate([slot_probs, jnp.zeros((slots, LANE - 1), jnp.bfloat16)], axis=1)
    send_t = jnp.concatenate([slot_tokens, prob_block], axis=1).reshape(exp_count, capacity, -1)
    arrived_t = exchange(send_t).reshape(slots, -1)
    send_g = slot_grads.reshape(exp_count, capacity, -1)
    arrived_g = exchange(send_g).reshape(slots, -1)

    stacked = jnp.concatenate([w_gate, w_up, w_down], axis=0)
    full = lax.all_gather(stacked, "rh", axis=1, tiled=True)
    gate_w = full[0]
    up_w = full[1]
    down_w = full[2]

    def block(arrived_rows, grads):
        rows = arrived_rows[:, :width]
        weight = arrived_rows[:, width : width + 1].astype(jnp.float32)
        gate = jnp.dot(rows, gate_w.T, preferred_element_type=jnp.float32)
        up = jnp.dot(rows, up_w.T, preferred_element_type=jnp.float32)
        sig = jax.nn.sigmoid(gate)
        act = gate * sig
        hidden = act * up
        back = jnp.dot(grads, down_w.T, preferred_element_type=jnp.float32)
        prob_part = jnp.sum(hidden * back, axis=1, keepdims=True)
        d_gate = (weight * back * up * sig * (1.0 + gate * (1.0 - sig))).astype(jnp.bfloat16)
        d_up = (weight * back * act).astype(jnp.bfloat16)
        weighted = (weight * hidden).astype(jnp.bfloat16)
        partial_rows = jnp.dot(d_gate, gate_w, preferred_element_type=jnp.float32) + jnp.dot(
            d_up, up_w, preferred_element_type=jnp.float32
        )
        packed = jnp.concatenate(
            [
                partial_rows.astype(jnp.bfloat16),
                prob_part.astype(jnp.bfloat16),
                jnp.zeros((rows.shape[0], LANE - 1), jnp.bfloat16),
            ],
            axis=1,
        )
        local = jnp.stack(
            [
                jnp.dot(d_gate.T, rows, preferred_element_type=jnp.float32),
                jnp.dot(d_up.T, rows, preferred_element_type=jnp.float32),
                jnp.dot(weighted.T, grads, preferred_element_type=jnp.float32),
            ]
        )
        return packed, local

    partner_t = swap_pair(arrived_t)
    partner_g = swap_pair(arrived_g)
    packed_own, local_own = block(arrived_t, arrived_g)
    packed_partner, local_partner = block(partner_t, partner_g)
    received = swap_pair(packed_partner)
    weight_grads = lax.psum_scatter(
        (local_own + local_partner).astype(jnp.bfloat16), "rh", scatter_dimension=1, tiled=True
    ).astype(jnp.float32)
    summed = (packed_own.astype(jnp.float32) + received.astype(jnp.float32)).astype(jnp.bfloat16)
    returned = exchange(summed.reshape(exp_count, capacity, -1)).reshape(slots, -1)

    grad_tokens = jnp.dot(
        token_routing.T, returned[:, :width], preferred_element_type=jnp.float32
    ).astype(jnp.bfloat16)
    grad_probs = jnp.dot(
        routing.T, returned[:, width : width + 1], preferred_element_type=jnp.float32
    ).reshape(token_count, 2)
    return (grad_tokens, grad_probs, weight_grads[0:1], weight_grads[1:2], weight_grads[2:3])


def solution(mesh):
    exp_count = mesh.shape["exp"]
    rep_count = mesh.shape["rep"]
    view = Mesh(mesh.devices.reshape(exp_count // 2, 2, rep_count // 2, 2), ("ez", "ec", "rh", "rl"))
    rows_spec = P(("ez", "ec", "rh", "rl"), None)
    weight_spec = P(("ez", "ec"), ("rh", "rl"), None)
    in_specs = (rows_spec,) * 4 + (weight_spec,) * 3
    out_specs = (rows_spec, rows_spec, weight_spec, weight_spec, weight_spec)
    return jax.shard_map(shards, mesh=view, in_specs=in_specs, out_specs=out_specs, check_vma=False)
```

```python
import jax
import jax.numpy as jnp
from jax import lax
from jax.sharding import Mesh
from jax.sharding import PartitionSpec as P

LANE = 128


def swap_pair(value):
    return lax.ppermute(value, "rl", [(0, 1), (1, 0)])


def exchange(blocks):
    shape = blocks.shape
    split = blocks.reshape((lax.axis_size("ez"), lax.axis_size("ec")) + shape[1:])
    split = lax.all_to_all(split, "ez", split_axis=0, concat_axis=0, tiled=True)
    split = lax.all_to_all(split, "ec", split_axis=1, concat_axis=1, tiled=True)
    return split.reshape(shape)


def exchange_back(blocks):
    shape = blocks.shape
    split = blocks.reshape((lax.axis_size("ez"), lax.axis_size("ec")) + shape[1:])
    split = lax.all_to_all(split, "ec", split_axis=1, concat_axis=1, tiled=True)
    split = lax.all_to_all(split, "ez", split_axis=0, concat_axis=0, tiled=True)
    return split.reshape(shape)


def shards(tokens, grad_out, expert_ids, probs, w_gate, w_up, w_down):
    token_count = tokens.shape[0]
    width = tokens.shape[1]
    exp_count = lax.axis_size("ez") * lax.axis_size("ec")
    capacity = 5 * token_count // (2 * exp_count)
    slots = exp_count * capacity
    chosen = expert_ids.reshape(-1)
    onehot = (chosen[:, None] == jnp.arange(exp_count, dtype=jnp.int32)[None, :]).astype(jnp.int32)
    ranks = jnp.sum((jnp.cumsum(onehot, axis=0) - 1) * onehot, axis=1)
    slot_of = chosen * capacity + ranks
    routing = (slot_of[None, :] == jnp.arange(slots, dtype=jnp.int32)[:, None]).astype(jnp.bfloat16)
    token_routing = routing.reshape(slots, token_count, 2).sum(axis=2)
    prob_pairs = probs.reshape(-1, 1)

    slot_tokens = jnp.dot(token_routing, tokens, preferred_element_type=jnp.float32).astype(jnp.bfloat16)
    slot_grads = jnp.dot(token_routing, grad_out, preferred_element_type=jnp.float32).astype(jnp.bfloat16)
    slot_probs = jnp.dot(routing, prob_pairs, preferred_element_type=jnp.float32).astype(jnp.bfloat16)
    prob_block = jnp.concatenate([slot_probs, jnp.zeros((slots, LANE - 1), jnp.bfloat16)], axis=1)
    send_t = jnp.concatenate([slot_tokens, prob_block], axis=1).reshape(exp_count, capacity, -1)
    arrived_t = exchange(send_t).reshape(slots, -1)
    send_g = slot_grads.reshape(exp_count, capacity, -1)
    arrived_g = exchange(send_g).reshape(slots, -1)

    stacked = jnp.concatenate([w_gate, w_up, w_down], axis=0)
    full = lax.all_gather(stacked, "rh", axis=1, tiled=True)
    gate_w = full[0]
    up_w = full[1]
    down_w = full[2]

    def block(arrived_rows, grads):
        rows = arrived_rows[:, :width]
        weight = arrived_rows[:, width : width + 1].astype(jnp.float32)
        gate = jnp.dot(rows, gate_w.T, preferred_element_type=jnp.float32)
        up = jnp.dot(rows, up_w.T, preferred_element_type=jnp.float32)
        sig = jax.nn.sigmoid(gate)
        act = gate * sig
        hidden = act * up
        back = jnp.dot(grads, down_w.T, preferred_element_type=jnp.float32)
        prob_part = jnp.sum(hidden * back, axis=1, keepdims=True)
        d_gate = (weight * back * up * sig * (1.0 + gate * (1.0 - sig))).astype(jnp.bfloat16)
        d_up = (weight * back * act).astype(jnp.bfloat16)
        weighted = (weight * hidden).astype(jnp.bfloat16)
        partial_rows = jnp.dot(d_gate, gate_w, preferred_element_type=jnp.float32) + jnp.dot(
            d_up, up_w, preferred_element_type=jnp.float32
        )
        packed = jnp.concatenate(
            [
                partial_rows.astype(jnp.bfloat16),
                prob_part.astype(jnp.bfloat16),
                jnp.zeros((rows.shape[0], LANE - 1), jnp.bfloat16),
            ],
            axis=1,
        )
        local = jnp.stack(
            [
                jnp.dot(d_gate.T, rows, preferred_element_type=jnp.float32),
                jnp.dot(d_up.T, rows, preferred_element_type=jnp.float32),
                jnp.dot(weighted.T, grads, preferred_element_type=jnp.float32),
            ]
        )
        return packed, local

    partner_t = swap_pair(arrived_t)
    partner_g = swap_pair(arrived_g)
    packed_own, local_own = block(arrived_t, arrived_g)
    packed_partner, local_partner = block(partner_t, partner_g)
    received = swap_pair(packed_partner)
    weight_grads = lax.psum_scatter(
        (local_own + local_partner).astype(jnp.bfloat16), "rh", scatter_dimension=1, tiled=True
    ).astype(jnp.float32)
    summed = (packed_own.astype(jnp.float32) + received.astype(jnp.float32)).astype(jnp.bfloat16)
    returned = exchange_back(summed.reshape(exp_count, capacity, -1)).reshape(slots, -1)

    grad_tokens = jnp.dot(
        token_routing.T, returned[:, :width], preferred_element_type=jnp.float32
    ).astype(jnp.bfloat16)
    grad_probs = jnp.dot(
        routing.T, returned[:, width : width + 1], preferred_element_type=jnp.float32
    ).reshape(token_count, 2)
    return (grad_tokens, grad_probs, weight_grads[0:1], weight_grads[1:2], weight_grads[2:3])


def solution(mesh):
    exp_count = mesh.shape["exp"]
    rep_count = mesh.shape["rep"]
    view = Mesh(mesh.devices.reshape(exp_count // 2, 2, rep_count // 2, 2), ("ez", "ec", "rh", "rl"))
    rows_spec = P(("ez", "ec", "rh", "rl"), None)
    weight_spec = P(("ez", "ec"), ("rh", "rl"), None)
    in_specs = (rows_spec,) * 4 + (weight_spec,) * 3
    out_specs = (rows_spec, rows_spec, weight_spec, weight_spec, weight_spec)
    return jax.shard_map(shards, mesh=view, in_specs=in_specs, out_specs=out_specs, check_vma=False)
```
